32 devices in a mesh: blk: 16 (over z, y, x), mp: 2 (over core).
Axes of the slice: x: 2, y: 2, z: 4, core: 2. Of those that a mesh axis runs over, the one named last changes fastest.
Arguments:
- queries: bfloat16 [6144, 2560], P('blk', 'mp'), may hold values from -11 to 11
- keys: bfloat16 [2048, 2560], P('blk', 'mp'), may hold values from -11 to 11
- values: bfloat16 [2048, 2560], P('blk', 'mp'), may hold values from -6 to 6
- out_weight: bfloat16 [2560, 5120], P('mp'), may hold values from -0.125 to 0.125
Outputs:
- mixed: bfloat16 [6144, 5120], P('blk', 'mp')
The draws below stay inside these ranges and needn't reach their ends.
All inputs are finite; a program needn't handle non-finite values.
Results may differ from the reference program's by a relative error of at most 0.018.
Values may be sent and summed in bfloat16 or wider, within the bound.
No kernel may reach another device: no remote copies, remote signals or barrier semaphores. Data moves between devices by JAX's collectives and lax.ppermute only.
A program may use at most 64 MiB of HBM per device.

```python
import math
import jax
import jax.numpy as jnp
from jax import lax

D = 5120
H = 20
HS = 128
Q_DEV = 384
KV_DEV = 128
HEAD_FEATURES = 2560
NQ = 6144
VOLUME_TOKENS = 2048
N_MP = 2


def draw_queries(key, part):
    attention_output = jnp.clip(jax.random.normal(jax.random.fold_in(key, 1), (NQ, HEAD_FEATURES), jnp.float32), -6.0, 6.0)
    return attention_output.astype(jnp.bfloat16)


def draw_keys(key, part):
    attention_output = jnp.clip(jax.random.normal(jax.random.fold_in(key, 2), (VOLUME_TOKENS, HEAD_FEATURES), jnp.float32), -6.0, 6.0)
    return attention_output.astype(jnp.bfloat16)


def block_scale(key, extent, split, smallest, high):
    def one(dim, blocks):
        heights = jax.random.uniform(jax.random.fold_in(jax.random.fold_in(key, 6), dim), (blocks,), jnp.float32, smallest / len(split), high / len(split))
        return jnp.repeat(jnp.exp(heights), extent[dim] // blocks).reshape((-1,) + (1,) * (len(extent) - dim - 1))

    factor_of = one(*split[0])
    for cut in split[1:]:
        factor_of = factor_of * one(*cut)
    return factor_of


def noise(stream_key, extent, deviation, limit, pieces=(), kind=jnp.bfloat16):
    loudness = block_scale(stream_key, extent, pieces, -0.22, 0.18) if pieces else 1.0
    result = jax.random.normal(stream_key, extent, jnp.float32) * deviation * loudness
    return jnp.minimum(jnp.maximum(result, -limit), limit).astype(kind)


def setup_inputs(seed: int = 0) -> dict:
    key_list = jax.random.split(jax.random.key(seed), 5)
    queries = draw_queries(jax.random.fold_in(key_list[4], 71), 0)
    keys = draw_keys(jax.random.fold_in(key_list[4], 71), 0)
    values = noise(key_list[2], (VOLUME_TOKENS, HEAD_FEATURES), 1.0, 6.0, ((0, 16), (1, 2)))
    out_weight = noise(key_list[3], (HEAD_FEATURES, D), HEAD_FEATURES ** -0.5, 0.125, ((0, 2),))
    return {"queries": queries, "keys": keys, "values": values, "out_weight": out_weight}


def attend_block(query_rows, key_rows, value_rows):
    score_scale = 1.0 / math.sqrt(HS)
    query_heads = query_rows.astype(jnp.float32).reshape(query_rows.shape[0], H, HS)
    key_heads = key_rows.astype(jnp.float32).reshape(key_rows.shape[0], H, HS)
    value_heads = value_rows.astype(jnp.float32).reshape(value_rows.shape[0], H, HS)
    scores = jnp.einsum('qhd,khd->qhk', query_heads, key_heads) * score_scale
    row_max = lax.optimization_barrier(jnp.max(scores, axis=-1, keepdims=True))
    weights = jnp.exp(scores - row_max)
    total = lax.optimization_barrier(jnp.sum(weights, axis=-1))
    weights_bf = lax.optimization_barrier(weights.astype(jnp.bfloat16)).astype(jnp.float32)
    numerator = jnp.einsum('qhk,khd->qhd', weights_bf, value_heads)
    attended = numerator / total[:, :, None]
    return attended.reshape(query_rows.shape[0], HEAD_FEATURES).astype(jnp.bfloat16)

def projection_rows(attended, out_weight):
    group_width = HEAD_FEATURES // N_MP
    summed = jnp.zeros((attended.shape[0], D), jnp.float32)
    for group in range(N_MP):
        cols = attended[:, group * group_width:(group + 1) * group_width]
        rows_w = out_weight[group * group_width:(group + 1) * group_width, :]
        window_partial_sum = jnp.dot(cols, rows_w, preferred_element_type=jnp.float32)
        summed = summed + lax.optimization_barrier(window_partial_sum.astype(jnp.bfloat16)).astype(jnp.float32)
    return summed.astype(jnp.bfloat16)

def reference(queries, keys, values, out_weight):
    blocks = NQ // Q_DEV
    query_grid = queries.reshape(blocks, Q_DEV, HEAD_FEATURES)
    key_grid = keys.reshape(blocks, KV_DEV, HEAD_FEATURES)
    value_grid = values.reshape(blocks, KV_DEV, HEAD_FEATURES)

    def per_block(which_block):
        nearby = (which_block + jnp.arange(-2, 3, dtype=jnp.int32) + blocks) % blocks
        key_rows = jnp.take(key_grid, nearby, axis=0).reshape(5 * KV_DEV, HEAD_FEATURES)
        value_rows = jnp.take(value_grid, nearby, axis=0).reshape(5 * KV_DEV, HEAD_FEATURES)
        query_rows = lax.dynamic_index_in_dim(query_grid, which_block, 0, keepdims=False)
        return projection_rows(attend_block(query_rows, key_rows, value_rows), out_weight)
    attention_output = lax.map(per_block, jnp.arange(blocks, dtype=jnp.int32))
    return attention_output.reshape(NQ, D)
```

```python
import math

import jax
import jax.numpy as jnp
from jax import lax
from jax.sharding import PartitionSpec as P

HS = 128


def from_behind(value, axis, steps):
    count = lax.axis_size(axis)
    pairs = [(source, (source + steps) % count) for source in range(count)]
    return lax.ppermute(value, axis, pairs)


def fold_block(state, stacked_blocks, query_heads):
    running_max, running_sum, numerator = state
    head_count = query_heads.shape[1]
    key_heads = stacked_blocks[0].reshape(stacked_blocks.shape[1], head_count, HS)
    value_heads = stacked_blocks[1].reshape(stacked_blocks.shape[1], head_count, HS)
    scores = jnp.einsum("qhd,khd->qhk", query_heads, key_heads, preferred_element_type=jnp.float32)
    scores = scores * (1.0 / math.sqrt(HS))
    new_max = jnp.maximum(running_max, jnp.max(scores, axis=-1))
    rescale = jnp.exp(running_max - new_max)
    weights = jnp.exp(scores - new_max[:, :, None])
    new_sum = running_sum * rescale + jnp.sum(weights, axis=-1)
    product = jnp.einsum(
        "qhk,khd->qhd",
        weights.astype(jnp.bfloat16),
        value_heads,
        preferred_element_type=jnp.float32,
    )
    new_numerator = numerator * rescale[:, :, None] + product
    return (new_max, new_sum, new_numerator)


def on_device(queries, keys, values, out_weight):
    row_count = queries.shape[0]
    head_count = queries.shape[1] // HS
    query_heads = queries.reshape(row_count, head_count, HS)
    state = (
        jnp.full((row_count, head_count), -jnp.inf, jnp.float32),
        jnp.zeros((row_count, head_count), jnp.float32),
        jnp.zeros((row_count, head_count, HS), jnp.float32),
    )
    stacked_blocks = jnp.stack((keys, values))
    arrivals = [from_behind(stacked_blocks, "blk", steps) for steps in (1, -1, 2, -2)]
    state = fold_block(state, stacked_blocks, query_heads)
    for moving in arrivals:
        state = fold_block(state, moving, query_heads)
    running_max, running_sum, numerator = state
    attended = (
        (numerator / running_sum[:, :, None])
        .reshape(row_count, head_count * HS)
        .astype(jnp.bfloat16)
    )
    window_partial_sum = jnp.dot(attended, out_weight, preferred_element_type=jnp.float32)
    summed = lax.psum_scatter(
        window_partial_sum.astype(jnp.bfloat16), "mp", scatter_dimension=1, tiled=True
    )
    return summed


def solution(mesh):
    placed = (P("blk", "mp"), P("blk", "mp"), P("blk", "mp"), P("mp", None))
    return jax.shard_map(
        on_device, mesh=mesh, in_specs=placed, out_specs=P("blk", "mp"), check_vma=False
    )
```

```python
import math

import jax
import jax.numpy as jnp
from jax import lax
from jax.sharding import PartitionSpec as P

HS = 128


def from_behind(value, axis, steps):
    count = lax.axis_size(axis)
    pairs = [(source, (source + steps) % count) for source in range(count)]
    return lax.ppermute(value, axis, pairs)


def fold_block(state, stacked_blocks, query_heads):
    running_max, running_sum, numerator = state
    head_count = query_heads.shape[1]
    key_heads = stacked_blocks[0].reshape(stacked_blocks.shape[1], head_count, HS)
    value_heads = stacked_blocks[1].reshape(stacked_blocks.shape[1], head_count, HS)
    scores = jnp.einsum("qhd,khd->qhk", query_heads, key_heads, preferred_element_type=jnp.float32)
    scores = scores * (1.0 / math.sqrt(HS))
    new_max = jnp.maximum(running_max, jnp.max(scores, axis=-1))
    rescale = jnp.exp(running_max - new_max)
    weights = jnp.exp(scores - new_max[:, :, None])
    new_sum = running_sum * rescale + jnp.sum(weights, axis=-1)
    product = jnp.einsum(
        "qhk,khd->qhd",
        weights.astype(jnp.bfloat16),
        value_heads,
        preferred_element_type=jnp.float32,
    )
    new_numerator = numerator * rescale[:, :, None] + product
    return (new_max, new_sum, new_numerator)


def on_device(queries, keys, values, out_weight):
    row_count = queries.shape[0]
    head_count = queries.shape[1] // HS
    query_heads = queries.reshape(row_count, head_count, HS)
    state = (
        jnp.full((row_count, head_count), -jnp.inf, jnp.float32),
        jnp.zeros((row_count, head_count), jnp.float32),
        jnp.zeros((row_count, head_count, HS), jnp.float32),
    )
    stacked_blocks = jnp.stack((keys, values))
    arrivals = [from_behind(stacked_blocks, "blk", steps) for steps in (1, -1, 2, -2)]
    state = fold_block(state, stacked_blocks, query_heads)
    for moving in arrivals:
        state = fold_block(state, moving, query_heads)
    running_max, running_sum, numerator = state
    attended = (
        (numerator / running_sum[:, :, None])
        .reshape(row_count, head_count * HS)
        .astype(jnp.bfloat16)
    )
    groups = lax.axis_size("mp")
    me = lax.axis_index("mp")
    width = out_weight.shape[1] // groups
    weight_cols = out_weight.reshape(out_weight.shape[0], groups, width)

    def partial_for(owner):
        cols = lax.dynamic_index_in_dim(weight_cols, owner, 1, keepdims=False)
        return jnp.dot(attended, cols, preferred_element_type=jnp.float32).astype(jnp.bfloat16)

    received = []
    for offset in range(1, groups):
        sent = partial_for((me + offset) % groups)
        pairs = [(source, (source + offset) % groups) for source in range(groups)]
        received.append(lax.ppermute(sent, "mp", pairs))
    summed = lax.optimization_barrier(partial_for(me)).astype(jnp.float32)
    for part in received:
        summed = summed + part.astype(jnp.float32)
    return summed.astype(jnp.bfloat16)


def solution(mesh):
    placed = (P("blk", "mp"), P("blk", "mp"), P("blk", "mp"), P("mp", None))
    return jax.shard_map(
        on_device, mesh=mesh, in_specs=placed, out_specs=P("blk", "mp"), check_vma=False
    )
```

```python
import math

import jax
import jax.numpy as jnp
from jax import lax
from jax.sharding import PartitionSpec as P

HS = 128


def swap_within_four(value, bit):
    count = lax.axis_size("blk")
    return lax.ppermute(value, "blk", [(source, source ^ bit) for source in range(count)])


def shift_groups(value):
    count = lax.axis_size("blk")
    groups = count // 4
    pairs = []
    for source in range(count):
        group, position = divmod(source, 4)
        step = 1 if position < 2 else -1
        pairs.append((source, ((group + step) % groups) * 4 + position))
    return lax.ppermute(value, "blk", pairs)


def relay_blocks(own):
    position = lax.axis_index("blk") % 4
    from_x = swap_within_four(own, 1)
    from_y = swap_within_four(own, 2)
    from_z = shift_groups(from_y)
    forward = jnp.where((position == 0) | (position == 3), from_y, from_z)
    from_last = swap_within_four(forward, 1)
    return [from_x, from_y, from_z, from_last]


def fold_block(state, key_rows, value_rows, query_heads):
    running_max, running_sum, numerator = state
    head_count = query_heads.shape[1]
    key_heads = key_rows.reshape(key_rows.shape[0], head_count, HS)
    value_heads = value_rows.reshape(value_rows.shape[0], head_count, HS)
    scores = jnp.einsum("qhd,khd->qhk", query_heads, key_heads, preferred_element_type=jnp.float32)
    scores = scores * (1.0 / math.sqrt(HS))
    new_max = jnp.maximum(running_max, jnp.max(scores, axis=-1))
    rescale = jnp.exp(running_max - new_max)
    weights = jnp.exp(scores - new_max[:, :, None])
    new_sum = running_sum * rescale + jnp.sum(weights, axis=-1)
    product = jnp.einsum(
        "qhk,khd->qhd",
        weights.astype(jnp.bfloat16),
        value_heads,
        preferred_element_type=jnp.float32,
    )
    new_numerator = numerator * rescale[:, :, None] + product
    return (new_max, new_sum, new_numerator)


def on_device(queries, keys, values, out_weight):
    row_count = queries.shape[0]
    head_count = queries.shape[1] // HS
    query_heads = queries.reshape(row_count, head_count, HS)
    state = (
        jnp.full((row_count, head_count), -jnp.inf, jnp.float32),
        jnp.zeros((row_count, head_count), jnp.float32),
        jnp.zeros((row_count, head_count, HS), jnp.float32),
    )
    key_arrivals = relay_blocks(keys)
    value_arrivals = relay_blocks(values)
    state = fold_block(state, keys, values, query_heads)
    for key_rows, value_rows in zip(key_arrivals, value_arrivals):
        state = fold_block(state, key_rows, value_rows, query_heads)
    running_max, running_sum, numerator = state
    attended = (
        (numerator / running_sum[:, :, None])
        .reshape(row_count, head_count * HS)
        .astype(jnp.bfloat16)
    )
    groups = lax.axis_size("mp")
    me = lax.axis_index("mp")
    width = out_weight.shape[1] // groups

    def partial_for(owner):
        cols = lax.dynamic_slice_in_dim(out_weight, owner * width, width, axis=1)
        return jnp.dot(attended, cols, preferred_element_type=jnp.float32).astype(jnp.bfloat16)

    received = []
    for offset in range(1, groups):
        sent = partial_for((me + offset) % groups)
        pairs = [(source, (source + offset) % groups) for source in range(groups)]
        received.append(lax.ppermute(sent, "mp", pairs))
    summed = lax.optimization_barrier(partial_for(me)).astype(jnp.float32)
    for part in received:
        summed = summed + part.astype(jnp.float32)
    return summed.astype(jnp.bfloat16)


def solution(mesh):
    placed = (P("blk", "mp"), P("blk", "mp"), P("blk", "mp"), P("mp", None))
    return jax.shard_map(
        on_device, mesh=mesh, in_specs=placed, out_specs=P("blk", "mp"), check_vma=False
    )
```

```python
import math

import jax
import jax.numpy as jnp
from jax import lax
from jax.sharding import PartitionSpec as P

HS = 128


def swap_within_four(value, bit):
    count = lax.axis_size("blk")
    return lax.ppermute(value, "blk", [(source, source ^ bit) for source in range(count)])


def shift_groups(value):
    count = lax.axis_size("blk")
    groups = count // 4
    pairs = []
    for source in range(count):
        group, position = divmod(source, 4)
        step = 1 if position < 2 else -1
        pairs.append((source, ((group + step) % groups) * 4 + position))
    return lax.ppermute(value, "blk", pairs)


def relay_blocks(own):
    position = lax.axis_index("blk") % 4
    from_x = swap_within_four(own, 1)
    from_y = swap_within_four(own, 2)
    from_z = shift_groups(from_y)
    forward = jnp.where((position == 0) | (position == 3), from_y, from_z)
    from_last = swap_within_four(forward, 1)
    return [from_x, from_y, from_z, from_last]


def fold_block(state, key_rows, value_rows, query_heads):
    running_max, running_sum, numerator = state
    head_count = query_heads.shape[1]
    key_heads = key_rows.reshape(key_rows.shape[0], head_count, HS)
    value_heads = value_rows.reshape(value_rows.shape[0], head_count, HS)
    scores = jnp.einsum("qhd,khd->qhk", query_heads, key_heads, preferred_element_type=jnp.float32)
    scores = scores * (1.0 / math.sqrt(HS))
    new_max = jnp.maximum(running_max, jnp.max(scores, axis=-1))
    rescale = jnp.exp(running_max - new_max)
    weights = jnp.exp(scores - new_max[:, :, None])
    new_sum = running_sum * rescale + jnp.sum(weights, axis=-1)
    product = jnp.einsum(
        "qhk,khd->qhd",
        weights.astype(jnp.bfloat16),
        value_heads,
        preferred_element_type=jnp.float32,
    )
    new_numerator = numerator * rescale[:, :, None] + product
    return (new_max, new_sum, new_numerator)


def attend_chunk(queries, keys, values, low, high, hold=None):
    row_count = queries.shape[0]
    cols = slice(low * HS, high * HS)
    count = high - low
    query_heads = queries[:, cols].reshape(row_count, count, HS)
    own = jnp.stack((keys[:, cols], values[:, cols]))
    state = (
        jnp.full((row_count, count), -jnp.inf, jnp.float32),
        jnp.zeros((row_count, count), jnp.float32),
        jnp.zeros((row_count, count, HS), jnp.float32),
    )
    state = fold_block(state, own[0], own[1], query_heads)
    arrivals = relay_blocks(own)
    for moving in arrivals[:-1]:
        state = fold_block(state, moving[0], moving[1], query_heads)
    last = arrivals[-1]
    if hold is not None:
        last, state, hold = lax.optimization_barrier((last, state, hold))
    state = fold_block(state, last[0], last[1], query_heads)
    running_max, running_sum, numerator = state
    attended = (
        (numerator / running_sum[:, :, None])
        .reshape(row_count, count * HS)
        .astype(jnp.bfloat16)
    )
    return attended, hold


def project_chunk(attended, weight_rows, owners, width):
    parts = []
    for owner in owners:
        block = lax.dynamic_slice_in_dim(weight_rows, owner * width, width, axis=1)
        parts.append(jnp.dot(attended, block, preferred_element_type=jnp.float32))
    return parts


def on_device(queries, keys, values, out_weight):
    head_count = queries.shape[1] // HS
    first = (head_count + 1) // 2
    groups = lax.axis_size("mp")
    me = lax.axis_index("mp")
    width = out_weight.shape[1] // groups
    owners = [(me + offset) % groups for offset in range(groups)]
    attended, _ = attend_chunk(queries, keys, values, 0, first)
    early = project_chunk(attended, out_weight[: first * HS], owners, width)
    attended, early = attend_chunk(queries, keys, values, first, head_count, hold=early)
    late = project_chunk(attended, out_weight[first * HS:], owners, width)
    totals = [a + b for a, b in zip(early, late)]
    received = []
    for offset in range(1, groups):
        pairs = [(source, (source + offset) % groups) for source in range(groups)]
        received.append(lax.ppermute(totals[offset].astype(jnp.bfloat16), "mp", pairs))
    summed = lax.optimization_barrier(totals[0].astype(jnp.bfloat16)).astype(jnp.float32)
    for part in received:
        summed = summed + part.astype(jnp.float32)
    return summed.astype(jnp.bfloat16)


def solution(mesh):
    placed = (P("blk", "mp"), P("blk", "mp"), P("blk", "mp"), P("mp", None))
    return jax.shard_map(
        on_device, mesh=mesh, in_specs=placed, out_specs=P("blk", "mp"), check_vma=False
    )
```

```python
import math

import jax
import jax.numpy as jnp
from jax import lax
from jax.sharding import PartitionSpec as P

HS = 128


def swap_within_four(value, bit):
    count = lax.axis_size("blk")
    return lax.ppermute(value, "blk", [(source, source ^ bit) for source in range(count)])


def shift_groups(value):
    count = lax.axis_size("blk")
    groups = count // 4
    pairs = []
    for source in range(count):
        group, position = divmod(source, 4)
        step = 1 if position < 2 else -1
        pairs.append((source, ((group + step) % groups) * 4 + position))
    return lax.ppermute(value, "blk", pairs)


def relay_stages(own):
    position = lax.axis_index("blk") % 4
    from_x = swap_within_four(own, 1)
    from_y = swap_within_four(own, 2)
    from_z = shift_groups(from_y)
    forward = jnp.where((position == 0) | (position == 3), from_y, from_z)
    return [from_x, from_y, from_z], forward


def fold_block(state, key_rows, value_rows, query_heads):
    running_max, running_sum, numerator = state
    head_count = query_heads.shape[1]
    key_heads = key_rows.reshape(key_rows.shape[0], head_count, HS)
    value_heads = value_rows.reshape(value_rows.shape[0], head_count, HS)
    scores = jnp.einsum("qhd,khd->qhk", query_heads, key_heads, preferred_element_type=jnp.float32)
    scores = scores * (1.0 / math.sqrt(HS))
    new_max = jnp.maximum(running_max, jnp.max(scores, axis=-1))
    rescale = jnp.exp(running_max - new_max)
    weights = jnp.exp(scores - new_max[:, :, None])
    new_sum = running_sum * rescale + jnp.sum(weights, axis=-1)
    product = jnp.einsum(
        "qhk,khd->qhd",
        weights.astype(jnp.bfloat16),
        value_heads,
        preferred_element_type=jnp.float32,
    )
    new_numerator = numerator * rescale[:, :, None] + product
    return (new_max, new_sum, new_numerator)


def on_device(queries, keys, values, out_weight):
    row_count = queries.shape[0]
    head_count = queries.shape[1] // HS
    query_heads = queries.reshape(row_count, head_count, HS)
    state = (
        jnp.full((row_count, head_count), -jnp.inf, jnp.float32),
        jnp.zeros((row_count, head_count), jnp.float32),
        jnp.zeros((row_count, head_count, HS), jnp.float32),
    )
    key_early, key_forward = relay_stages(keys)
    value_early, value_forward = relay_stages(values)
    key_last = swap_within_four(key_forward, 1)
    value_last = swap_within_four(value_forward, 1)
    _, *held = lax.optimization_barrier(
        (value_forward, keys, values, *key_early, *value_early)
    )
    key_blocks = [held[0]] + held[2:5] + [key_last]
    value_blocks = [held[1]] + held[5:8] + [value_last]
    for key_rows, value_rows in zip(key_blocks, value_blocks):
        state = fold_block(state, key_rows, value_rows, query_heads)
    running_max, running_sum, numerator = state
    attended = (
        (numerator / running_sum[:, :, None])
        .reshape(row_count, head_count * HS)
        .astype(jnp.bfloat16)
    )
    groups = lax.axis_size("mp")
    me = lax.axis_index("mp")
    width = out_weight.shape[1] // groups

    def partial_for(owner):
        cols = lax.dynamic_slice_in_dim(out_weight, owner * width, width, axis=1)
        return jnp.dot(attended, cols, preferred_element_type=jnp.float32).astype(jnp.bfloat16)

    received = []
    for offset in range(1, groups):
        sent = partial_for((me + offset) % groups)
        pairs = [(source, (source + offset) % groups) for source in range(groups)]
        received.append(lax.ppermute(sent, "mp", pairs))
    summed = lax.optimization_barrier(partial_for(me)).astype(jnp.float32)
    for part in received:
        summed = summed + part.astype(jnp.float32)
    return summed.astype(jnp.bfloat16)


def solution(mesh):
    placed = (P("blk", "mp"), P("blk", "mp"), P("blk", "mp"), P("mp", None))
    return jax.shard_map(
        on_device, mesh=mesh, in_specs=placed, out_specs=P("blk", "mp"), check_vma=False
    )
```

```python
import math

import jax
import jax.numpy as jnp
from jax import lax
from jax.sharding import PartitionSpec as P

HS = 128


def swap_within_four(value, bit):
    count = lax.axis_size("blk")
    return lax.ppermute(value, "blk", [(source, source ^ bit) for source in range(count)])


def shift_groups(value):
    count = lax.axis_size("blk")
    groups = count // 4
    pairs = []
    for source in range(count):
        group, position = divmod(source, 4)
        step = 1 if position < 2 else -1
        pairs.append((source, ((group + step) % groups) * 4 + position))
    return lax.ppermute(value, "blk", pairs)


def relay_pair(keys, values):
    position = lax.axis_index("blk") % 4
    key_x = swap_within_four(keys, 1)
    value_x = swap_within_four(values, 1)
    key_y = swap_within_four(keys, 2)
    values, _ = lax.optimization_barrier((values, key_y))
    value_y = swap_within_four(values, 2)
    key_z = shift_groups(key_y)
    value_z = shift_groups(value_y)
    keep = (position == 0) | (position == 3)
    key_last = swap_within_four(jnp.where(keep, key_y, key_z), 1)
    value_last = swap_within_four(jnp.where(keep, value_y, value_z), 1)
    return [(key_x, value_x), (key_y, value_y), (key_z, value_z), (key_last, value_last)]


def fold_block(state, key_rows, value_rows, query_heads):
    running_max, running_sum, numerator = state
    head_count = query_heads.shape[1]
    key_heads = key_rows.reshape(key_rows.shape[0], head_count, HS)
    value_heads = value_rows.reshape(value_rows.shape[0], head_count, HS)
    scores = jnp.einsum("qhd,khd->qhk", query_heads, key_heads, preferred_element_type=jnp.float32)
    scores = scores * (1.0 / math.sqrt(HS))
    new_max = jnp.maximum(running_max, jnp.max(scores, axis=-1))
    rescale = jnp.exp(running_max - new_max)
    weights = jnp.exp(scores - new_max[:, :, None])
    new_sum = running_sum * rescale + jnp.sum(weights, axis=-1)
    product = jnp.einsum(
        "qhk,khd->qhd",
        weights.astype(jnp.bfloat16),
        value_heads,
        preferred_element_type=jnp.float32,
    )
    new_numerator = numerator * rescale[:, :, None] + product
    return (new_max, new_sum, new_numerator)


def on_device(queries, keys, values, out_weight):
    row_count = queries.shape[0]
    head_count = queries.shape[1] // HS
    query_heads = queries.reshape(row_count, head_count, HS)
    state = (
        jnp.full((row_count, head_count), -jnp.inf, jnp.float32),
        jnp.zeros((row_count, head_count), jnp.float32),
        jnp.zeros((row_count, head_count, HS), jnp.float32),
    )
    arrivals = relay_pair(keys, values)
    state = fold_block(state, keys, values, query_heads)
    for key_rows, value_rows in arrivals:
        state = fold_block(state, key_rows, value_rows, query_heads)
    running_max, running_sum, numerator = state
    attended = (
        (numerator / running_sum[:, :, None])
        .reshape(row_count, head_count * HS)
        .astype(jnp.bfloat16)
    )
    groups = lax.axis_size("mp")
    me = lax.axis_index("mp")
    width = out_weight.shape[1] // groups

    def partial_for(owner):
        cols = lax.dynamic_slice_in_dim(out_weight, owner * width, width, axis=1)
        return jnp.dot(attended, cols, preferred_element_type=jnp.float32).astype(jnp.bfloat16)

    received = []
    for offset in range(1, groups):
        sent = partial_for((me + offset) % groups)
        pairs = [(source, (source + offset) % groups) for source in range(groups)]
        received.append(lax.ppermute(sent, "mp", pairs))
    summed = lax.optimization_barrier(partial_for(me)).astype(jnp.float32)
    for part in received:
        summed = summed + part.astype(jnp.float32)
    return summed.astype(jnp.bfloat16)


def solution(mesh):
    placed = (P("blk", "mp"), P("blk", "mp"), P("blk", "mp"), P("mp", None))
    return jax.shard_map(
        on_device, mesh=mesh, in_specs=placed, out_specs=P("blk", "mp"), check_vma=False
    )
```

```python
import math

import jax
import jax.numpy as jnp
from jax import lax
from jax.experimental import pallas as pl
from jax.experimental.pallas import tpu as pltpu
from jax.sharding import PartitionSpec as P

HS = 128


def swap_within_four(value, bit):
    count = lax.axis_size("blk")
    return lax.ppermute(value, "blk", [(source, source ^ bit) for source in range(count)])


def shift_groups(value):
    count = lax.axis_size("blk")
    groups = count // 4
    pairs = []
    for source in range(count):
        group, position = divmod(source, 4)
        step = 1 if position < 2 else -1
        pairs.append((source, ((group + step) % groups) * 4 + position))
    return lax.ppermute(value, "blk", pairs)


def relay_blocks(own):
    position = lax.axis_index("blk") % 4
    from_x = swap_within_four(own, 1)
    from_y = swap_within_four(own, 2)
    from_z = shift_groups(from_y)
    forward = jnp.where((position == 0) | (position == 3), from_y, from_z)
    from_last = swap_within_four(forward, 1)
    return [from_x, from_y, from_z, from_last]


def window_kernel(*refs):
    blocks = (len(refs) - 2) // 2
    q_ref = refs[0]
    key_refs = refs[1:1 + blocks]
    value_refs = refs[1 + blocks:1 + 2 * blocks]
    out_ref = refs[-1]
    head_count = q_ref.shape[1] // HS
    scale = 1.0 / math.sqrt(HS)
    for head in range(head_count):
        cols = pl.ds(head * HS, HS)
        query = q_ref[:, cols]
        scores = [
            lax.dot_general(query, k[:, cols], (((1,), (1,)), ((), ())),
                            preferred_element_type=jnp.float32) * scale
            for k in key_refs
        ]
        row_max = scores[0].max(axis=1, keepdims=True)
        for s in scores[1:]:
            row_max = jnp.maximum(row_max, s.max(axis=1, keepdims=True))
        total = None
        numerator = None
        for s, v in zip(scores, value_refs):
            weights = jnp.exp(s - row_max)
            part_sum = weights.sum(axis=1, keepdims=True)
            total = part_sum if total is None else total + part_sum
            product = jnp.dot(weights.astype(jnp.bfloat16), v[:, cols],
                              preferred_element_type=jnp.float32)
            numerator = product if numerator is None else numerator + product
        out_ref[:, cols] = (numerator / total).astype(out_ref.dtype)


def attend_window(queries, key_blocks, value_blocks):
    rows, width = queries.shape
    blocks = len(key_blocks)
    kv = key_blocks[0].shape[0]
    flops = 4 * rows * kv * blocks * width
    return pl.pallas_call(
        window_kernel,
        out_shape=jax.ShapeDtypeStruct((rows, width), jnp.bfloat16),
        in_specs=[pl.BlockSpec(memory_space=pltpu.VMEM)] * (1 + 2 * blocks),
        out_specs=pl.BlockSpec(memory_space=pltpu.VMEM),
        cost_estimate=pl.CostEstimate(
            flops=flops,
            transcendentals=rows * kv * blocks * (width // HS),
            bytes_accessed=2 * (2 * rows * width + 2 * blocks * kv * width),
        ),
    )(queries, *key_blocks, *value_blocks)


def on_device(queries, keys, values, out_weight):
    key_blocks = [keys] + relay_blocks(keys)
    value_blocks = [values] + relay_blocks(values)
    attended = attend_window(queries, key_blocks, value_blocks)
    groups = lax.axis_size("mp")
    me = lax.axis_index("mp")
    width = out_weight.shape[1] // groups

    def partial_for(owner):
        cols = lax.dynamic_slice_in_dim(out_weight, owner * width, width, axis=1)
        return jnp.dot(attended, cols, preferred_element_type=jnp.float32).astype(jnp.bfloat16)

    received = []
    for offset in range(1, groups):
        sent = partial_for((me + offset) % groups)
        pairs = [(source, (source + offset) % groups) for source in range(groups)]
        received.append(lax.ppermute(sent, "mp", pairs))
    summed = lax.optimization_barrier(partial_for(me)).astype(jnp.float32)
    for part in received:
        summed = summed + part.astype(jnp.float32)
    return summed.astype(jnp.bfloat16)


def solution(mesh):
    placed = (P("blk", "mp"), P("blk", "mp"), P("blk", "mp"), P("mp", None))
    return jax.shard_map(
        on_device, mesh=mesh, in_specs=placed, out_specs=P("blk", "mp"), check_vma=False
    )
```

```python
import math

import jax
import jax.numpy as jnp
from jax import lax
from jax.sharding import PartitionSpec as P

HS = 128


def swap_within_four(value, bit):
    count = lax.axis_size("blk")
    return lax.ppermute(value, "blk", [(source, source ^ bit) for source in range(count)])


def shift_groups(value):
    count = lax.axis_size("blk")
    groups = count // 4
    pairs = []
    for source in range(count):
        group, position = divmod(source, 4)
        step = 1 if position < 2 else -1
        pairs.append((source, ((group + step) % groups) * 4 + position))
    return lax.ppermute(value, "blk", pairs)


def relay_blocks(own):
    position = lax.axis_index("blk") % 4
    from_x = swap_within_four(own, 1)
    from_y = swap_within_four(own, 2)
    from_z = shift_groups(from_y)
    forward = jnp.where((position == 0) | (position == 3), from_y, from_z)
    from_last = swap_within_four(forward, 1)
    return [from_x, from_y, from_z, from_last]


def fold_block(state, key_rows, value_rows, query_heads):
    running_max, running_sum, numerator = state
    head_count = query_heads.shape[1]
    key_heads = key_rows.reshape(key_rows.shape[0], head_count, HS)
    value_heads = value_rows.reshape(value_rows.shape[0], head_count, HS)
    scores = jnp.einsum("qhd,khd->qhk", query_heads, key_heads, preferred_element_type=jnp.float32)
    scores = scores * (1.0 / math.sqrt(HS))
    new_max = jnp.maximum(running_max, jnp.max(scores, axis=-1))
    rescale = jnp.exp(running_max - new_max)
    weights = jnp.exp(scores - new_max[:, :, None])
    new_sum = running_sum * rescale + jnp.sum(weights, axis=-1)
    product = jnp.einsum(
        "qhk,khd->qhd",
        weights.astype(jnp.bfloat16),
        value_heads,
        preferred_element_type=jnp.float32,
    )
    new_numerator = numerator * rescale[:, :, None] + product
    return (new_max, new_sum, new_numerator)


def on_device(queries, keys, values, out_weight):
    row_count = queries.shape[0]
    head_count = queries.shape[1] // HS
    query_heads = queries.reshape(row_count, head_count, HS)
    state = (
        jnp.full((row_count, head_count), -jnp.inf, jnp.float32),
        jnp.zeros((row_count, head_count), jnp.float32),
        jnp.zeros((row_count, head_count, HS), jnp.float32),
    )
    key_arrivals = relay_blocks(keys)
    value_arrivals = relay_blocks(values)
    state = fold_block(state, keys, values, query_heads)
    for key_rows, value_rows in zip(key_arrivals, value_arrivals):
        state = fold_block(state, key_rows, value_rows, query_heads)
    running_max, running_sum, numerator = state
    attended = (
        (numerator / running_sum[:, :, None])
        .reshape(row_count, head_count * HS)
        .astype(jnp.bfloat16)
    )
    groups = lax.axis_size("mp")
    me = lax.axis_index("mp")
    width = out_weight.shape[1] // groups

    def columns_of(weight, owner):
        return lax.dynamic_slice_in_dim(weight, owner * width, width, axis=1)

    def project(rows, weight_cols):
        return jnp.dot(rows, weight_cols, preferred_element_type=jnp.float32).astype(jnp.bfloat16)

    summed = lax.optimization_barrier(project(attended, columns_of(out_weight, me))).astype(jnp.float32)
    for offset in range(1, groups):
        pairs = [(source, (source + offset) % groups) for source in range(groups)]
        weight_cols = lax.ppermute(columns_of(out_weight, (me + offset) % groups), "mp", pairs)
        rows = lax.ppermute(attended, "mp", pairs)
        summed = summed + project(rows, weight_cols).astype(jnp.float32)
    return summed.astype(jnp.bfloat16)


def solution(mesh):
    placed = (P("blk", "mp"), P("blk", "mp"), P("blk", "mp"), P("mp", None))
    return jax.shard_map(
        on_device, mesh=mesh, in_specs=placed, out_specs=P("blk", "mp"), check_vma=False
    )
```

```python
import math

import jax
import jax.numpy as jnp
from jax import lax
from jax.experimental.layout import Layout, with_layout_constraint
from jax.sharding import PartitionSpec as P

HS = 128


def swap_within_four(value, bit):
    count = lax.axis_size("blk")
    return lax.ppermute(value, "blk", [(source, source ^ bit) for source in range(count)])


def shift_groups(value):
    count = lax.axis_size("blk")
    groups = count // 4
    pairs = []
    for source in range(count):
        group, position = divmod(source, 4)
        step = 1 if position < 2 else -1
        pairs.append((source, ((group + step) % groups) * 4 + position))
    return lax.ppermute(value, "blk", pairs)


def relay_blocks(own):
    position = lax.axis_index("blk") % 4
    from_x = swap_within_four(own, 1)
    from_y = swap_within_four(own, 2)
    from_z = shift_groups(from_y)
    forward = jnp.where((position == 0) | (position == 3), from_y, from_z)
    from_last = swap_within_four(forward, 1)
    return [from_x, from_y, from_z, from_last]


def fold_block(state, key_rows, value_rows, query_heads):
    running_max, running_sum, numerator = state
    head_count = query_heads.shape[1]
    key_heads = key_rows.reshape(key_rows.shape[0], head_count, HS)
    value_heads = value_rows.reshape(value_rows.shape[0], head_count, HS)
    scores = jnp.einsum("qhd,khd->qhk", query_heads, key_heads, preferred_element_type=jnp.float32)
    scores = scores * (1.0 / math.sqrt(HS))
    new_max = jnp.maximum(running_max, jnp.max(scores, axis=-1))
    rescale = jnp.exp(running_max - new_max)
    weights = jnp.exp(scores - new_max[:, :, None])
    new_sum = running_sum * rescale + jnp.sum(weights, axis=-1)
    product = jnp.einsum(
        "qhk,khd->qhd",
        weights.astype(jnp.bfloat16),
        value_heads,
        preferred_element_type=jnp.float32,
    )
    new_numerator = numerator * rescale[:, :, None] + product
    return (new_max, new_sum, new_numerator)


def on_device(queries, keys, values, out_weight):
    row_count = queries.shape[0]
    head_count = queries.shape[1] // HS
    query_heads = queries.reshape(row_count, head_count, HS)
    state = (
        jnp.full((row_count, head_count), -jnp.inf, jnp.float32),
        jnp.zeros((row_count, head_count), jnp.float32),
        jnp.zeros((row_count, head_count, HS), jnp.float32),
    )
    keys = with_layout_constraint(keys, Layout(major_to_minor=(1, 0)))
    values = with_layout_constraint(values, Layout(major_to_minor=(1, 0)))
    key_arrivals = relay_blocks(keys)
    value_arrivals = relay_blocks(values)
    state = fold_block(state, keys, values, query_heads)
    for key_rows, value_rows in zip(key_arrivals, value_arrivals):
        state = fold_block(state, key_rows, value_rows, query_heads)
    running_max, running_sum, numerator = state
    attended = (
        (numerator / running_sum[:, :, None])
        .reshape(row_count, head_count * HS)
        .astype(jnp.bfloat16)
    )
    groups = lax.axis_size("mp")
    me = lax.axis_index("mp")
    width = out_weight.shape[1] // groups

    def partial_for(owner):
        cols = lax.dynamic_slice_in_dim(out_weight, owner * width, width, axis=1)
        return jnp.dot(attended, cols, preferred_element_type=jnp.float32).astype(jnp.bfloat16)

    received = []
    for offset in range(1, groups):
        sent = partial_for((me + offset) % groups)
        pairs = [(source, (source + offset) % groups) for source in range(groups)]
        received.append(lax.ppermute(sent, "mp", pairs))
    summed = lax.optimization_barrier(partial_for(me)).astype(jnp.float32)
    for part in received:
        summed = summed + part.astype(jnp.float32)
    return summed.astype(jnp.bfloat16)


def solution(mesh):
    placed = (P("blk", "mp"), P("blk", "mp"), P("blk", "mp"), P("mp", None))
    return jax.shard_map(
        on_device, mesh=mesh, in_specs=placed, out_specs=P("blk", "mp"), check_vma=False
    )
```

```python
import math

import jax
import jax.numpy as jnp
from jax import lax
from jax.experimental.layout import Layout, with_layout_constraint
from jax.sharding import PartitionSpec as P

HS = 128


def swap_within_four(value, bit):
    count = lax.axis_size("blk")
    return lax.ppermute(value, "blk", [(source, source ^ bit) for source in range(count)])


def shift_groups(value):
    count = lax.axis_size("blk")
    groups = count // 4
    pairs = []
    for source in range(count):
        group, position = divmod(source, 4)
        step = 1 if position < 2 else -1
        pairs.append((source, ((group + step) % groups) * 4 + position))
    return lax.ppermute(value, "blk", pairs)


def relay_chain(own):
    position = lax.axis_index("blk") % 4
    from_y = swap_within_four(own, 2)
    from_z = shift_groups(from_y)
    forward = jnp.where((position == 0) | (position == 3), from_y, from_z)
    from_last = swap_within_four(forward, 1)
    return [from_y, from_z, from_last]


def fold_block(state, key_rows, value_rows, query_heads):
    running_max, running_sum, numerator = state
    head_count = query_heads.shape[1]
    key_heads = key_rows.reshape(key_rows.shape[0], head_count, HS)
    value_heads = value_rows.reshape(value_rows.shape[0], head_count, HS)
    scores = jnp.einsum("qhd,khd->qhk", query_heads, key_heads, preferred_element_type=jnp.float32)
    scores = scores * (1.0 / math.sqrt(HS))
    new_max = jnp.maximum(running_max, jnp.max(scores, axis=-1))
    rescale = jnp.exp(running_max - new_max)
    weights = jnp.exp(scores - new_max[:, :, None])
    new_sum = running_sum * rescale + jnp.sum(weights, axis=-1)
    product = jnp.einsum(
        "qhk,khd->qhd",
        weights.astype(jnp.bfloat16),
        value_heads,
        preferred_element_type=jnp.float32,
    )
    new_numerator = numerator * rescale[:, :, None] + product
    return (new_max, new_sum, new_numerator)


def on_device(queries, keys, values, out_weight):
    row_count = queries.shape[0]
    head_count = queries.shape[1] // HS
    query_heads = queries.reshape(row_count, head_count, HS)
    state = (
        jnp.full((row_count, head_count), -jnp.inf, jnp.float32),
        jnp.zeros((row_count, head_count), jnp.float32),
        jnp.zeros((row_count, head_count, HS), jnp.float32),
    )
    keys = with_layout_constraint(keys, Layout(major_to_minor=(1, 0)))
    values = with_layout_constraint(values, Layout(major_to_minor=(1, 0)))
    from_x = swap_within_four(jnp.stack((keys, values)), 1)
    key_arrivals = [from_x[0]] + relay_chain(keys)
    value_arrivals = [from_x[1]] + relay_chain(values)
    state = fold_block(state, keys, values, query_heads)
    for key_rows, value_rows in zip(key_arrivals, value_arrivals):
        state = fold_block(state, key_rows, value_rows, query_heads)
    running_max, running_sum, numerator = state
    attended = (
        (numerator / running_sum[:, :, None])
        .reshape(row_count, head_count * HS)
        .astype(jnp.bfloat16)
    )
    groups = lax.axis_size("mp")
    me = lax.axis_index("mp")
    width = out_weight.shape[1] // groups

    def partial_for(owner):
        cols = lax.dynamic_slice_in_dim(out_weight, owner * width, width, axis=1)
        return jnp.dot(attended, cols, preferred_element_type=jnp.float32).astype(jnp.bfloat16)

    received = []
    for offset in range(1, groups):
        sent = partial_for((me + offset) % groups)
        pairs = [(source, (source + offset) % groups) for source in range(groups)]
        received.append(lax.ppermute(sent, "mp", pairs))
    summed = lax.optimization_barrier(partial_for(me)).astype(jnp.float32)
    for part in received:
        summed = summed + part.astype(jnp.float32)
    return summed.astype(jnp.bfloat16)


def solution(mesh):
    placed = (P("blk", "mp"), P("blk", "mp"), P("blk", "mp"), P("mp", None))
    return jax.shard_map(
        on_device, mesh=mesh, in_specs=placed, out_specs=P("blk", "mp"), check_vma=False
    )
```

```python
import math

import jax
import jax.numpy as jnp
from jax import lax
from jax.experimental.layout import Layout, with_layout_constraint
from jax.sharding import PartitionSpec as P

HS = 128


def swap_within_four(value, bit):
    count = lax.axis_size("blk")
    return lax.ppermute(value, "blk", [(source, source ^ bit) for source in range(count)])


def shift_groups(value):
    count = lax.axis_size("blk")
    groups = count // 4
    pairs = []
    for source in range(count):
        group, position = divmod(source, 4)
        step = 1 if position < 2 else -1
        pairs.append((source, ((group + step) % groups) * 4 + position))
    return lax.ppermute(value, "blk", pairs)


def relay_chain(own):
    position = lax.axis_index("blk") % 4
    from_y = swap_within_four(own, 2)
    from_z = shift_groups(from_y)
    forward = jnp.where((position == 0) | (position == 3), from_y, from_z)
    from_last = swap_within_four(forward, 1)
    return [from_y, from_z, from_last]


def fold_block(state, key_rows, value_rows, query_heads):
    running_max, running_sum, numerator = state
    head_count = query_heads.shape[1]
    key_heads = key_rows.reshape(key_rows.shape[0], head_count, HS)
    value_heads = value_rows.reshape(value_rows.shape[0], head_count, HS)
    scores = jnp.einsum("qhd,khd->qhk", query_heads, key_heads, preferred_element_type=jnp.float32)
    scores = scores * (1.0 / math.sqrt(HS))
    new_max = jnp.maximum(running_max, jnp.max(scores, axis=-1))
    rescale = jnp.exp(running_max - new_max)
    weights = jnp.exp(scores - new_max[:, :, None])
    new_sum = running_sum * rescale + jnp.sum(weights, axis=-1)
    product = jnp.einsum(
        "qhk,khd->qhd",
        weights.astype(jnp.bfloat16),
        value_heads,
        preferred_element_type=jnp.float32,
    )
    new_numerator = numerator * rescale[:, :, None] + product
    return (new_max, new_sum, new_numerator)


def on_device(queries, keys, values, out_weight):
    row_count = queries.shape[0]
    head_count = queries.shape[1] // HS
    query_heads = queries.reshape(row_count, head_count, HS)
    state = (
        jnp.full((row_count, head_count), -jnp.inf, jnp.float32),
        jnp.zeros((row_count, head_count), jnp.float32),
        jnp.zeros((row_count, head_count, HS), jnp.float32),
    )
    keys = with_layout_constraint(keys, Layout(major_to_minor=(1, 0)))
    values = with_layout_constraint(values, Layout(major_to_minor=(1, 0)))
    from_x = swap_within_four(jnp.stack((keys, values)), 1)
    key_arrivals = [from_x[0]] + relay_chain(keys)
    value_arrivals = [from_x[1]] + relay_chain(values)
    state = fold_block(state, keys, values, query_heads)
    for index, (key_rows, value_rows) in enumerate(zip(key_arrivals, value_arrivals)):
        if index < 2:
            state = lax.optimization_barrier(state)
        state = fold_block(state, key_rows, value_rows, query_heads)
    running_max, running_sum, numerator = state
    attended = (
        (numerator / running_sum[:, :, None])
        .reshape(row_count, head_count * HS)
        .astype(jnp.bfloat16)
    )
    groups = lax.axis_size("mp")
    me = lax.axis_index("mp")
    width = out_weight.shape[1] // groups

    def partial_for(owner):
        cols = lax.dynamic_slice_in_dim(out_weight, owner * width, width, axis=1)
        return jnp.dot(attended, cols, preferred_element_type=jnp.float32).astype(jnp.bfloat16)

    received = []
    for offset in range(1, groups):
        sent = partial_for((me + offset) % groups)
        pairs = [(source, (source + offset) % groups) for source in range(groups)]
        received.append(lax.ppermute(sent, "mp", pairs))
    summed = lax.optimization_barrier(partial_for(me)).astype(jnp.float32)
    for part in received:
        summed = summed + part.astype(jnp.float32)
    return summed.astype(jnp.bfloat16)


def solution(mesh):
    placed = (P("blk", "mp"), P("blk", "mp"), P("blk", "mp"), P("mp", None))
    return jax.shard_map(
        on_device, mesh=mesh, in_specs=placed, out_specs=P("blk", "mp"), check_vma=False
    )
```

```python
import math

import jax
import jax.numpy as jnp
from jax import lax
from jax.experimental.layout import Layout, with_layout_constraint
from jax.sharding import PartitionSpec as P

HS = 128


def swap_within_four(value, bit):
    count = lax.axis_size("blk")
    return lax.ppermute(value, "blk", [(source, source ^ bit) for source in range(count)])


def shift_groups(value):
    count = lax.axis_size("blk")
    groups = count // 4
    pairs = []
    for source in range(count):
        group, position = divmod(source, 4)
        step = 1 if position < 2 else -1
        pairs.append((source, ((group + step) % groups) * 4 + position))
    return lax.ppermute(value, "blk", pairs)


def relay_chain(own, stored=False):
    def hold(value):
        return with_layout_constraint(value, Layout(major_to_minor=(0, 1))) if stored else value

    position = lax.axis_index("blk") % 4
    from_y = hold(swap_within_four(hold(own), 2))
    from_z = hold(shift_groups(from_y))
    forward = hold(jnp.where((position == 0) | (position == 3), from_y, from_z))
    from_last = hold(swap_within_four(forward, 1))
    return [from_y, from_z, from_last]


def fold_block(state, key_rows, value_rows, query_heads):
    running_max, running_sum, numerator = state
    head_count = query_heads.shape[1]
    key_heads = key_rows.reshape(key_rows.shape[0], head_count, HS)
    value_heads = value_rows.reshape(value_rows.shape[0], head_count, HS)
    scores = jnp.einsum("qhd,khd->qhk", query_heads, key_heads, preferred_element_type=jnp.float32)
    scores = scores * (1.0 / math.sqrt(HS))
    new_max = jnp.maximum(running_max, jnp.max(scores, axis=-1))
    rescale = jnp.exp(running_max - new_max)
    weights = jnp.exp(scores - new_max[:, :, None])
    new_sum = running_sum * rescale + jnp.sum(weights, axis=-1)
    product = jnp.einsum(
        "qhk,khd->qhd",
        weights.astype(jnp.bfloat16),
        value_heads,
        preferred_element_type=jnp.float32,
    )
    new_numerator = numerator * rescale[:, :, None] + product
    return (new_max, new_sum, new_numerator)


def on_device(queries, keys, values, out_weight):
    row_count = queries.shape[0]
    head_count = queries.shape[1] // HS
    query_heads = queries.reshape(row_count, head_count, HS)
    state = (
        jnp.full((row_count, head_count), -jnp.inf, jnp.float32),
        jnp.zeros((row_count, head_count), jnp.float32),
        jnp.zeros((row_count, head_count, HS), jnp.float32),
    )
    key_chain = relay_chain(keys, stored=True)
    keys = with_layout_constraint(keys, Layout(major_to_minor=(1, 0)))
    values = with_layout_constraint(values, Layout(major_to_minor=(1, 0)))
    from_x = swap_within_four(jnp.stack((keys, values)), 1)
    key_arrivals = [from_x[0]] + key_chain
    value_arrivals = [from_x[1]] + relay_chain(values)
    state = fold_block(state, keys, values, query_heads)
    for key_rows, value_rows in zip(key_arrivals, value_arrivals):
        state = fold_block(state, key_rows, value_rows, query_heads)
    running_max, running_sum, numerator = state
    attended = (
        (numerator / running_sum[:, :, None])
        .reshape(row_count, head_count * HS)
        .astype(jnp.bfloat16)
    )
    groups = lax.axis_size("mp")
    me = lax.axis_index("mp")
    width = out_weight.shape[1] // groups

    def partial_for(owner):
        cols = lax.dynamic_slice_in_dim(out_weight, owner * width, width, axis=1)
        return jnp.dot(attended, cols, preferred_element_type=jnp.float32).astype(jnp.bfloat16)

    received = []
    for offset in range(1, groups):
        sent = partial_for((me + offset) % groups)
        pairs = [(source, (source + offset) % groups) for source in range(groups)]
        received.append(lax.ppermute(sent, "mp", pairs))
    summed = lax.optimization_barrier(partial_for(me)).astype(jnp.float32)
    for part in received:
        summed = summed + part.astype(jnp.float32)
    return summed.astype(jnp.bfloat16)


def solution(mesh):
    placed = (P("blk", "mp"), P("blk", "mp"), P("blk", "mp"), P("mp", None))
    return jax.shard_map(
        on_device, mesh=mesh, in_specs=placed, out_specs=P("blk", "mp"), check_vma=False
    )
```

```python
import math

import jax
import jax.numpy as jnp
from jax import lax
from jax.experimental.layout import Layout, with_layout_constraint
from jax.sharding import PartitionSpec as P

HS = 128


def swap_within_four(value, bit):
    count = lax.axis_size("blk")
    return lax.ppermute(value, "blk", [(source, source ^ bit) for source in range(count)])


def shift_groups(value):
    count = lax.axis_size("blk")
    groups = count // 4
    pairs = []
    for source in range(count):
        group, position = divmod(source, 4)
        step = 1 if position < 2 else -1
        pairs.append((source, ((group + step) % groups) * 4 + position))
    return lax.ppermute(value, "blk", pairs)


def swap_pairs(value, pairs):
    count = lax.axis_size("blk")
    return lax.ppermute(
        value, "blk", [(s, s ^ 1) for s in range(count) if (s % 4) in pairs]
    )


def relay_chain(own):
    position = lax.axis_index("blk") % 4
    from_y = swap_within_four(own, 2)
    from_z = shift_groups(from_y)
    last_via_y = swap_pairs(from_y, (0, 3))
    last_via_z = swap_pairs(from_z, (1, 2))
    from_last = jnp.where((position == 1) | (position == 2), last_via_y, last_via_z)
    return [from_y, from_z, from_last]


def fold_block(state, key_rows, value_rows, query_heads):
    running_max, running_sum, numerator = state
    head_count = query_heads.shape[1]
    key_heads = key_rows.reshape(key_rows.shape[0], head_count, HS)
    value_heads = value_rows.reshape(value_rows.shape[0], head_count, HS)
    scores = jnp.einsum("qhd,khd->qhk", query_heads, key_heads, preferred_element_type=jnp.float32)
    scores = scores * (1.0 / math.sqrt(HS))
    new_max = jnp.maximum(running_max, jnp.max(scores, axis=-1))
    rescale = jnp.exp(running_max - new_max)
    weights = jnp.exp(scores - new_max[:, :, None])
    new_sum = running_sum * rescale + jnp.sum(weights, axis=-1)
    product = jnp.einsum(
        "qhk,khd->qhd",
        weights.astype(jnp.bfloat16),
        value_heads,
        preferred_element_type=jnp.float32,
    )
    new_numerator = numerator * rescale[:, :, None] + product
    return (new_max, new_sum, new_numerator)


def on_device(queries, keys, values, out_weight):
    row_count = queries.shape[0]
    head_count = queries.shape[1] // HS
    query_heads = queries.reshape(row_count, head_count, HS)
    state = (
        jnp.full((row_count, head_count), -jnp.inf, jnp.float32),
        jnp.zeros((row_count, head_count), jnp.float32),
        jnp.zeros((row_count, head_count, HS), jnp.float32),
    )
    keys = with_layout_constraint(keys, Layout(major_to_minor=(1, 0)))
    values = with_layout_constraint(values, Layout(major_to_minor=(1, 0)))
    from_x = swap_within_four(jnp.stack((keys, values)), 1)
    key_arrivals = [from_x[0]] + relay_chain(keys)
    value_arrivals = [from_x[1]] + relay_chain(values)
    state = fold_block(state, keys, values, query_heads)
    for key_rows, value_rows in zip(key_arrivals, value_arrivals):
        state = fold_block(state, key_rows, value_rows, query_heads)
    running_max, running_sum, numerator = state
    attended = (
        (numerator / running_sum[:, :, None])
        .reshape(row_count, head_count * HS)
        .astype(jnp.bfloat16)
    )
    groups = lax.axis_size("mp")
    me = lax.axis_index("mp")
    width = out_weight.shape[1] // groups

    def partial_for(owner):
        cols = lax.dynamic_slice_in_dim(out_weight, owner * width, width, axis=1)
        return jnp.dot(attended, cols, preferred_element_type=jnp.float32).astype(jnp.bfloat16)

    received = []
    for offset in range(1, groups):
        sent = partial_for((me + offset) % groups)
        pairs = [(source, (source + offset) % groups) for source in range(groups)]
        received.append(lax.ppermute(sent, "mp", pairs))
    summed = lax.optimization_barrier(partial_for(me)).astype(jnp.float32)
    for part in received:
        summed = summed + part.astype(jnp.float32)
    return summed.astype(jnp.bfloat16)


def solution(mesh):
    placed = (P("blk", "mp"), P("blk", "mp"), P("blk", "mp"), P("mp", None))
    return jax.shard_map(
        on_device, mesh=mesh, in_specs=placed, out_specs=P("blk", "mp"), check_vma=False
    )
```

```python
import math

import jax
import jax.numpy as jnp
from jax import lax
from jax.experimental.layout import Layout, with_layout_constraint
from jax.sharding import PartitionSpec as P

HS = 128


def swap_within_four(value, bit):
    count = lax.axis_size("blk")
    return lax.ppermute(value, "blk", [(source, source ^ bit) for source in range(count)])


def shift_groups(value):
    count = lax.axis_size("blk")
    groups = count // 4
    pairs = []
    for source in range(count):
        group, position = divmod(source, 4)
        step = 1 if position < 2 else -1
        pairs.append((source, ((group + step) % groups) * 4 + position))
    return lax.ppermute(value, "blk", pairs)


def relay_chain(own):
    position = lax.axis_index("blk") % 4
    from_y = swap_within_four(own, 2)
    from_z = shift_groups(from_y)
    forward = jnp.where((position == 0) | (position == 3), from_y, from_z)
    from_last = swap_within_four(forward, 1)
    return [from_y, from_z, from_last]


def fold_block(state, key_rows, value_rows, query_heads):
    running_max, running_sum, numerator = state
    head_count = query_heads.shape[1]
    key_heads = key_rows.reshape(key_rows.shape[0], head_count, HS)
    value_heads = value_rows.reshape(value_rows.shape[0], head_count, HS)
    scores = jnp.einsum("qhd,khd->qhk", query_heads, key_heads, preferred_element_type=jnp.float32)
    scores = scores * (1.0 / math.sqrt(HS))
    new_max = jnp.maximum(running_max, jnp.max(scores, axis=-1))
    rescale = jnp.exp(running_max - new_max)
    weights = jnp.exp(scores - new_max[:, :, None])
    new_sum = running_sum * rescale + jnp.sum(weights, axis=-1)
    product = jnp.einsum(
        "qhk,khd->qhd",
        weights.astype(jnp.bfloat16),
        value_heads,
        preferred_element_type=jnp.float32,
    )
    new_numerator = numerator * rescale[:, :, None] + product
    return (new_max, new_sum, new_numerator)


def on_device(queries, keys, values, out_weight):
    row_count = queries.shape[0]
    head_count = queries.shape[1] // HS
    query_heads = queries.reshape(row_count, head_count, HS)
    state = (
        jnp.full((row_count, head_count), -jnp.inf, jnp.float32),
        jnp.zeros((row_count, head_count), jnp.float32),
        jnp.zeros((row_count, head_count, HS), jnp.float32),
    )
    keys = with_layout_constraint(keys, Layout(major_to_minor=(1, 0)))
    values = with_layout_constraint(values, Layout(major_to_minor=(1, 0)))
    from_x = swap_within_four(jnp.stack((keys, values)), 1)
    key_arrivals = [from_x[0]] + relay_chain(keys)
    value_arrivals = [from_x[1]] + relay_chain(values)
    blocks = list(zip(key_arrivals, value_arrivals))
    blocks.insert(3, (keys, values))
    for key_rows, value_rows in blocks:
        state = fold_block(state, key_rows, value_rows, query_heads)
    running_max, running_sum, numerator = state
    attended = (
        (numerator / running_sum[:, :, None])
        .reshape(row_count, head_count * HS)
        .astype(jnp.bfloat16)
    )
    groups = lax.axis_size("mp")
    me = lax.axis_index("mp")
    width = out_weight.shape[1] // groups

    def partial_for(owner):
        cols = lax.dynamic_slice_in_dim(out_weight, owner * width, width, axis=1)
        return jnp.dot(attended, cols, preferred_element_type=jnp.float32).astype(jnp.bfloat16)

    received = []
    for offset in range(1, groups):
        sent = partial_for((me + offset) % groups)
        pairs = [(source, (source + offset) % groups) for source in range(groups)]
        received.append(lax.ppermute(sent, "mp", pairs))
    summed = lax.optimization_barrier(partial_for(me)).astype(jnp.float32)
    for part in received:
        summed = summed + part.astype(jnp.float32)
    return summed.astype(jnp.bfloat16)


def solution(mesh):
    placed = (P("blk", "mp"), P("blk", "mp"), P("blk", "mp"), P("mp", None))
    return jax.shard_map(
        on_device, mesh=mesh, in_specs=placed, out_specs=P("blk", "mp"), check_vma=False
    )
```

```python
import math

import jax
import jax.numpy as jnp
from jax import lax
from jax.experimental.layout import Layout, with_layout_constraint
from jax.sharding import PartitionSpec as P

HS = 128


def swap_within_four(value, bit):
    count = lax.axis_size("blk")
    return lax.ppermute(value, "blk", [(source, source ^ bit) for source in range(count)])


def shift_groups(value):
    count = lax.axis_size("blk")
    groups = count // 4
    pairs = []
    for source in range(count):
        group, position = divmod(source, 4)
        step = 1 if position < 2 else -1
        pairs.append((source, ((group + step) % groups) * 4 + position))
    return lax.ppermute(value, "blk", pairs)


def relay_chain(own):
    position = lax.axis_index("blk") % 4
    from_y = swap_within_four(own, 2)
    from_z = shift_groups(from_y)
    forward = jnp.where((position == 0) | (position == 3), from_y, from_z)
    from_last = swap_within_four(forward, 1)
    return [from_y, from_z, from_last]


def fold_block(state, key_rows, value_rows, query_heads):
    running_max, running_sum, numerator = state
    head_count = query_heads.shape[1]
    key_heads = key_rows.reshape(key_rows.shape[0], head_count, HS)
    value_heads = value_rows.reshape(value_rows.shape[0], head_count, HS)
    scores = jnp.einsum("qhd,khd->qhk", query_heads, key_heads, preferred_element_type=jnp.float32)
    scores = scores * (1.0 / math.sqrt(HS))
    new_max = jnp.maximum(running_max, jnp.max(scores, axis=-1))
    rescale = jnp.exp(running_max - new_max)
    weights = jnp.exp(scores - new_max[:, :, None])
    new_sum = running_sum * rescale + jnp.sum(weights, axis=-1)
    product = jnp.einsum(
        "qhk,khd->qhd",
        weights.astype(jnp.bfloat16),
        value_heads,
        preferred_element_type=jnp.float32,
    )
    new_numerator = numerator * rescale[:, :, None] + product
    return (new_max, new_sum, new_numerator)


def on_device(queries, keys, values, out_weight):
    row_count = queries.shape[0]
    head_count = queries.shape[1] // HS
    query_heads = queries.reshape(row_count, head_count, HS)
    state = (
        jnp.full((row_count, head_count), -jnp.inf, jnp.float32),
        jnp.zeros((row_count, head_count), jnp.float32),
        jnp.zeros((row_count, head_count, HS), jnp.float32),
    )
    keys = with_layout_constraint(keys, Layout(major_to_minor=(1, 0)))
    values = with_layout_constraint(values, Layout(major_to_minor=(1, 0)))
    width = keys.shape[1]
    from_x = swap_within_four(jnp.concatenate((keys, values), axis=1), 1)
    key_arrivals = [from_x[:, :width]] + relay_chain(keys)
    value_arrivals = [from_x[:, width:]] + relay_chain(values)
    state = fold_block(state, keys, values, query_heads)
    for key_rows, value_rows in zip(key_arrivals, value_arrivals):
        state = fold_block(state, key_rows, value_rows, query_heads)
    running_max, running_sum, numerator = state
    attended = (
        (numerator / running_sum[:, :, None])
        .reshape(row_count, head_count * HS)
        .astype(jnp.bfloat16)
    )
    groups = lax.axis_size("mp")
    me = lax.axis_index("mp")
    width = out_weight.shape[1] // groups

    def partial_for(owner):
        cols = lax.dynamic_slice_in_dim(out_weight, owner * width, width, axis=1)
        return jnp.dot(attended, cols, preferred_element_type=jnp.float32).astype(jnp.bfloat16)

    received = []
    for offset in range(1, groups):
        sent = partial_for((me + offset) % groups)
        pairs = [(source, (source + offset) % groups) for source in range(groups)]
        received.append(lax.ppermute(sent, "mp", pairs))
    summed = lax.optimization_barrier(partial_for(me)).astype(jnp.float32)
    for part in received:
        summed = summed + part.astype(jnp.float32)
    return summed.astype(jnp.bfloat16)


def solution(mesh):
    placed = (P("blk", "mp"), P("blk", "mp"), P("blk", "mp"), P("mp", None))
    return jax.shard_map(
        on_device, mesh=mesh, in_specs=placed, out_specs=P("blk", "mp"), check_vma=False
    )
```

```python
import math

import jax
import jax.numpy as jnp
from jax import lax
from jax.experimental.layout import Layout, with_layout_constraint
from jax.sharding import PartitionSpec as P

HS = 128


def swap_within_four(value, bit):
    count = lax.axis_size("blk")
    return lax.ppermute(value, "blk", [(source, source ^ bit) for source in range(count)])


def shift_groups(value):
    count = lax.axis_size("blk")
    groups = count // 4
    pairs = []
    for source in range(count):
        group, position = divmod(source, 4)
        step = 1 if position < 2 else -1
        pairs.append((source, ((group + step) % groups) * 4 + position))
    return lax.ppermute(value, "blk", pairs)


def relay_chain(own):
    position = lax.axis_index("blk") % 4
    from_y = swap_within_four(own, 2)
    from_z = shift_groups(from_y)
    forward = jnp.where((position == 0) | (position == 3), from_y, from_z)
    from_last = swap_within_four(forward, 1)
    return [from_y, from_z, from_last]


def fold_block(state, key_rows, value_rows, query_heads):
    running_max, running_sum, numerator = state
    head_count = query_heads.shape[1]
    key_heads = key_rows.reshape(key_rows.shape[0], head_count, HS)
    value_heads = value_rows.reshape(value_rows.shape[0], head_count, HS)
    scores = jnp.einsum("qhd,khd->qhk", query_heads, key_heads, preferred_element_type=jnp.float32)
    scores = scores * (1.0 / math.sqrt(HS))
    new_max = jnp.maximum(running_max, jnp.max(scores, axis=-1))
    rescale = jnp.exp(running_max - new_max)
    weights = jnp.exp(scores - new_max[:, :, None])
    new_sum = running_sum * rescale + jnp.sum(weights, axis=-1)
    product = jnp.einsum(
        "qhk,khd->qhd",
        weights.astype(jnp.bfloat16),
        value_heads,
        preferred_element_type=jnp.float32,
    )
    new_numerator = numerator * rescale[:, :, None] + product
    return (new_max, new_sum, new_numerator)


def on_device(queries, keys, values, out_weight):
    row_count = queries.shape[0]
    head_count = queries.shape[1] // HS
    query_heads = queries.reshape(row_count, head_count, HS)
    keys = with_layout_constraint(keys, Layout(major_to_minor=(1, 0)))
    values = with_layout_constraint(values, Layout(major_to_minor=(1, 0)))
    from_x = swap_within_four(jnp.stack((keys, values)), 1)
    key_blocks = [keys, from_x[0]] + relay_chain(keys)
    value_blocks = [values, from_x[1]] + relay_chain(values)
    scores = [
        jnp.einsum(
            "qhd,khd->qhk",
            query_heads,
            k.reshape(k.shape[0], head_count, HS),
            preferred_element_type=jnp.float32,
        )
        * (1.0 / math.sqrt(HS))
        for k in key_blocks
    ]
    row_max = scores[0].max(axis=-1)
    for s in scores[1:]:
        row_max = jnp.maximum(row_max, s.max(axis=-1))
    total = None
    numerator = None
    for s, v in zip(scores, value_blocks):
        weights = jnp.exp(s - row_max[:, :, None])
        part = weights.sum(axis=-1)
        total = part if total is None else total + part
        product = jnp.einsum(
            "qhk,khd->qhd",
            weights.astype(jnp.bfloat16),
            v.reshape(v.shape[0], head_count, HS),
            preferred_element_type=jnp.float32,
        )
        numerator = product if numerator is None else numerator + product
    attended = (
        (numerator / total[:, :, None])
        .reshape(row_count, head_count * HS)
        .astype(jnp.bfloat16)
    )
    groups = lax.axis_size("mp")
    me = lax.axis_index("mp")
    width = out_weight.shape[1] // groups

    def partial_for(owner):
        cols = lax.dynamic_slice_in_dim(out_weight, owner * width, width, axis=1)
        return jnp.dot(attended, cols, preferred_element_type=jnp.float32).astype(jnp.bfloat16)

    received = []
    for offset in range(1, groups):
        sent = partial_for((me + offset) % groups)
        pairs = [(source, (source + offset) % groups) for source in range(groups)]
        received.append(lax.ppermute(sent, "mp", pairs))
    summed = lax.optimization_barrier(partial_for(me)).astype(jnp.float32)
    for part in received:
        summed = summed + part.astype(jnp.float32)
    return summed.astype(jnp.bfloat16)


def solution(mesh):
    placed = (P("blk", "mp"), P("blk", "mp"), P("blk", "mp"), P("mp", None))
    return jax.shard_map(
        on_device, mesh=mesh, in_specs=placed, out_specs=P("blk", "mp"), check_vma=False
    )
```

```python
import math

import jax
import jax.numpy as jnp
from jax import lax
from jax.experimental.layout import Layout, with_layout_constraint
from jax.sharding import PartitionSpec as P

HS = 128


def swap_within_four(value, bit):
    count = lax.axis_size("blk")
    return lax.ppermute(value, "blk", [(source, source ^ bit) for source in range(count)])


def shift_groups(value):
    count = lax.axis_size("blk")
    groups = count // 4
    pairs = []
    for source in range(count):
        group, position = divmod(source, 4)
        step = 1 if position < 2 else -1
        pairs.append((source, ((group + step) % groups) * 4 + position))
    return lax.ppermute(value, "blk", pairs)


def relay_chain(own):
    position = lax.axis_index("blk") % 4
    from_y = swap_within_four(own, 2)
    from_z = shift_groups(from_y)
    forward = jnp.where((position == 0) | (position == 3), from_y, from_z)
    from_last = swap_within_four(forward, 1)
    return [from_y, from_z, from_last]


def fold_block(state, key_rows, value_rows, query_heads):
    running_max, running_sum, numerator = state
    head_count = query_heads.shape[1]
    key_heads = key_rows.reshape(key_rows.shape[0], head_count, HS)
    value_heads = value_rows.reshape(value_rows.shape[0], head_count, HS)
    scores = jnp.einsum("qhd,khd->qhk", query_heads, key_heads, preferred_element_type=jnp.float32)
    scores = scores * (1.0 / math.sqrt(HS))
    new_max = jnp.maximum(running_max, jnp.max(scores, axis=-1))
    rescale = jnp.exp(running_max - new_max)
    weights = jnp.exp(scores - new_max[:, :, None])
    new_sum = running_sum * rescale + jnp.sum(weights, axis=-1)
    product = jnp.einsum(
        "qhk,khd->qhd",
        weights.astype(jnp.bfloat16),
        value_heads,
        preferred_element_type=jnp.float32,
    )
    new_numerator = numerator * rescale[:, :, None] + product
    return (new_max, new_sum, new_numerator)


def on_device(queries, keys, values, out_weight):
    row_count = queries.shape[0]
    head_count = queries.shape[1] // HS
    query_heads = queries.reshape(row_count, head_count, HS)
    state = (
        jnp.full((row_count, head_count), -jnp.inf, jnp.float32),
        jnp.zeros((row_count, head_count), jnp.float32),
        jnp.zeros((row_count, head_count, HS), jnp.float32),
    )
    keys = with_layout_constraint(keys, Layout(major_to_minor=(1, 0)))
    values = with_layout_constraint(values, Layout(major_to_minor=(1, 0)))
    from_x = swap_within_four(jnp.stack((keys, values)), 1)
    key_arrivals = [from_x[0]] + relay_chain(keys)
    value_arrivals = [from_x[1]] + relay_chain(values)
    state = fold_block(state, keys, values, query_heads)
    for key_rows, value_rows in zip(key_arrivals, value_arrivals):
        state = fold_block(state, key_rows, value_rows, query_heads)
    running_max, running_sum, numerator = state
    attended = (
        (numerator / running_sum[:, :, None])
        .reshape(row_count, head_count * HS)
        .astype(jnp.bfloat16)
    )
    groups = lax.axis_size("mp")
    me = lax.axis_index("mp")
    width = out_weight.shape[1] // groups

    def partial_for(owner):
        cols = lax.dynamic_slice_in_dim(out_weight, owner * width, width, axis=1)
        return jnp.dot(attended, cols, preferred_element_type=jnp.float32).astype(jnp.bfloat16)

    def half_for(owner, half):
        step = width // 2
        cols = lax.dynamic_slice_in_dim(out_weight, owner * width + half * step, step, axis=1)
        return jnp.dot(attended, cols, preferred_element_type=jnp.float32).astype(jnp.bfloat16)

    received = []
    for offset in range(1, groups):
        pairs = [(source, (source + offset) % groups) for source in range(groups)]
        halves = [lax.ppermute(half_for((me + offset) % groups, h), "mp", pairs) for h in (0, 1)]
        received.append(jnp.concatenate(halves, axis=1))
    summed = lax.optimization_barrier(partial_for(me)).astype(jnp.float32)
    for part in received:
        summed = summed + part.astype(jnp.float32)
    return summed.astype(jnp.bfloat16)


def solution(mesh):
    placed = (P("blk", "mp"), P("blk", "mp"), P("blk", "mp"), P("mp", None))
    return jax.shard_map(
        on_device, mesh=mesh, in_specs=placed, out_specs=P("blk", "mp"), check_vma=False
    )
```

```python
import math

import jax
import jax.numpy as jnp
from jax import lax
from jax.experimental.layout import Layout, with_layout_constraint
from jax.sharding import PartitionSpec as P

HS = 128


def swap_within_four(value, bit):
    count = lax.axis_size("blk")
    return lax.ppermute(value, "blk", [(source, source ^ bit) for source in range(count)])


def shift_groups(value):
    count = lax.axis_size("blk")
    groups = count // 4
    pairs = []
    for source in range(count):
        group, position = divmod(source, 4)
        step = 1 if position < 2 else -1
        pairs.append((source, ((group + step) % groups) * 4 + position))
    return lax.ppermute(value, "blk", pairs)


def relay_chain(own):
    position = lax.axis_index("blk") % 4
    from_y = swap_within_four(own, 2)
    from_z = shift_groups(from_y)
    forward = jnp.where((position == 0) | (position == 3), from_y, from_z)
    from_last = swap_within_four(forward, 1)
    return [from_y, from_z, from_last]


def fold_block(state, key_rows, value_rows, query_heads):
    running_max, running_sum, numerator = state
    head_count = query_heads.shape[1]
    key_heads = key_rows.reshape(key_rows.shape[0], head_count, HS)
    value_heads = value_rows.reshape(value_rows.shape[0], head_count, HS)
    scores = jnp.einsum("qhd,khd->qhk", query_heads, key_heads, preferred_element_type=jnp.float32)
    scores = scores * (1.0 / math.sqrt(HS))
    new_max = jnp.maximum(running_max, jnp.max(scores, axis=-1))
    rescale = jnp.exp(running_max - new_max)
    weights = jnp.exp(scores - new_max[:, :, None])
    new_sum = running_sum * rescale + jnp.sum(weights, axis=-1)
    product = jnp.einsum(
        "qhk,khd->qhd",
        weights.astype(jnp.bfloat16),
        value_heads,
        preferred_element_type=jnp.float32,
    )
    new_numerator = numerator * rescale[:, :, None] + product
    return (new_max, new_sum, new_numerator)


def on_device(queries, keys, values, out_weight):
    row_count = queries.shape[0]
    head_count = queries.shape[1] // HS
    query_heads = queries.reshape(row_count, head_count, HS)
    state = (
        jnp.full((row_count, head_count), -jnp.inf, jnp.float32),
        jnp.zeros((row_count, head_count), jnp.float32),
        jnp.zeros((row_count, head_count, HS), jnp.float32),
    )
    keys = with_layout_constraint(keys, Layout(major_to_minor=(1, 0)))
    values = with_layout_constraint(values, Layout(major_to_minor=(1, 0)))
    width = keys.shape[1]
    from_x = swap_within_four(jnp.concatenate((keys, values), axis=1), 1)
    key_arrivals = [from_x[:, :width]] + relay_chain(keys)
    value_arrivals = [from_x[:, width:]] + relay_chain(values)
    state = fold_block(state, keys, values, query_heads)
    for key_rows, value_rows in zip(key_arrivals, value_arrivals):
        state = fold_block(state, key_rows, value_rows, query_heads)
    running_max, running_sum, numerator = state
    attended = (
        (numerator / running_sum[:, :, None])
        .reshape(row_count, head_count * HS)
        .astype(jnp.bfloat16)
    )
    groups = lax.axis_size("mp")
    me = lax.axis_index("mp")
    width = out_weight.shape[1] // groups

    def partial_for(owner):
        cols = lax.dynamic_slice_in_dim(out_weight, owner * width, width, axis=1)
        return jnp.dot(attended, cols, preferred_element_type=jnp.float32).astype(jnp.bfloat16)

    def half_for(owner, half):
        step = width // 2
        cols = lax.dynamic_slice_in_dim(out_weight, owner * width + half * step, step, axis=1)
        return jnp.dot(attended, cols, preferred_element_type=jnp.float32).astype(jnp.bfloat16)

    received = []
    for offset in range(1, groups):
        pairs = [(source, (source + offset) % groups) for source in range(groups)]
        halves = [lax.ppermute(half_for((me + offset) % groups, h), "mp", pairs) for h in (0, 1)]
        received.append(jnp.concatenate(halves, axis=1))
    summed = lax.optimization_barrier(partial_for(me)).astype(jnp.float32)
    for part in received:
        summed = summed + part.astype(jnp.float32)
    return summed.astype(jnp.bfloat16)


def solution(mesh):
    placed = (P("blk", "mp"), P("blk", "mp"), P("blk", "mp"), P("mp", None))
    return jax.shard_map(
        on_device, mesh=mesh, in_specs=placed, out_specs=P("blk", "mp"), check_vma=False
    )
```
